128 devices in a mesh: group: 16 (over z, x), local: 8 (over y, core).
Axes of the slice: x: 4, y: 4, z: 4, core: 2. Of those that a mesh axis runs over, the one named last changes fastest.
Arguments:
- tokens: bfloat16 [2048, 3584], P(('group', 'local')), may hold values from -6 to 6
- expert_ids: int32 [2048, 8], P(('group', 'local')), may hold values from 0 to 127, as said below
- gate_codes: int32 [2048, 8], P(('group', 'local')), may hold values from 1 to 1024
- w_gate: bfloat16 [128, 3584, 1024], P(('group', 'local')), may hold values from -0.09375 to 0.09375
- w_up: bfloat16 [128, 3584, 1024], P(('group', 'local')), may hold values from -0.09375 to 0.09375
- w_down: bfloat16 [128, 1024, 3584], P(('group', 'local')), may hold values from -0.1875 to 0.1875
Outputs:
- mixed: bfloat16 [2048, 3584], P(('group', 'local'))
The draws below stay inside these ranges and needn't reach their ends.
Inputs may be any that keep to these rules, and one draw needn't show every extreme that they name: `expert_ids`: each row names 8 different experts, and they lie within at most 4 node groups, node group g holding experts g * 8 to (g + 1) * 8 - 1.
All inputs are finite; a program needn't handle non-finite values.
Results may differ from the reference program's by a relative error of at most 0.0057.
Values may be sent and summed in bfloat16 or wider, within the bound.
No kernel may reach another device: no remote copies, remote signals or barrier semaphores. Data moves between devices by JAX's collectives and lax.ppermute only.
A program may use at most 128 MiB of HBM per device.

```python
import jax
import jax.numpy as jnp
from jax import lax

D = 3584
H = 1024
TOPK = 8
TOPG = 4
TOK_DEV = 16
EXPERTS = 128
EXP_GROUP = 8
CAP = 2
TOKENS = 2048
N_GROUP = 16
N_LOCAL = 8


def draw_expert_ids(key, part):
    base = jax.random.fold_in(key, 11)
    key_pop, key_gpop, key_group, key_expert = jax.random.split(base, 4)
    groups = EXPERTS // EXP_GROUP
    popular = jax.random.randint(key_pop, (EXPERTS,), 1, 5)
    group_pop = jax.random.randint(key_gpop, (groups,), 1, 4)
    group_score = jax.random.randint(key_group, (TOKENS, groups), 0, 4096) * group_pop[None, :]
    group_score = group_score * groups + jnp.arange(groups, dtype=jnp.int32)[None, :]
    unused, chosen = lax.top_k(group_score, TOPG)
    group_range = jnp.arange(groups, dtype=jnp.int32)
    group_mask = jnp.any(chosen[:, :, None] == group_range[None, None, :], axis=1)
    expert_range = jnp.arange(EXPERTS, dtype=jnp.int32)
    allowed = group_mask[:, expert_range // EXP_GROUP]
    expert_score = jax.random.randint(key_expert, (TOKENS, EXPERTS), 0, 4096) * popular[None, :]
    expert_score = expert_score * EXPERTS + expert_range[None, :]
    expert_score = jnp.where(allowed, expert_score, -1 - expert_range[None, :])
    unused_two, picked = lax.top_k(expert_score, TOPK)
    return picked.astype(jnp.int32)


def touch_ends(values, stream_key, smallest, high):
    dims = values.shape
    spot = [jax.random.randint(jax.random.fold_in(stream_key, axis), (), 0, dims[axis]) for axis in range(len(dims))]
    values = values.at[tuple(spot)].set(smallest)
    longest = dims.index(max(dims))
    spot[longest] = (spot[longest] + 1) % dims[longest]
    return values.at[tuple(spot)].set(high)


def steps_of(own_key, extent, cuts, low, largest):
    def one(position, blocks):
        steps = jax.random.uniform(jax.random.fold_in(jax.random.fold_in(own_key, 6), position), (blocks,), jnp.float32, low / len(cuts), largest / len(cuts))
        return jnp.repeat(jnp.exp(steps), extent[position] // blocks).reshape((-1,) + (1,) * (len(extent) - position - 1))

    loudness = one(*cuts[0])
    for cut in cuts[1:]:
        loudness = loudness * one(*cut)
    return loudness


def centred(rng, extent, spread, reach, shards=(), held_as=jnp.bfloat16):
    values = spread * jax.random.normal(rng, extent, jnp.float32)
    if shards:
        values = values * steps_of(rng, extent, shards, -0.22, 0.18)
    return jnp.clip(values, -reach, reach).astype(held_as)


def setup_inputs(seed: int = 0) -> dict:
    key_list = jax.random.split(jax.random.key(seed), 7)
    return {
        "tokens": centred(key_list[0], (TOKENS, D), 1.0, 6.0, ((0, 128),)),
        "expert_ids": draw_expert_ids(jax.random.fold_in(key_list[6], 71), 0),
        "gate_codes": touch_ends(jax.random.randint(key_list[2], (TOKENS, TOPK), 1, 1025), jax.random.fold_in(key_list[2], 1), 1, 1024).astype(jnp.int32),
        "w_gate": centred(key_list[3], (EXPERTS, D, H), D ** -0.5, 0.09375, ((0, 128),)),
        "w_up": centred(key_list[4], (EXPERTS, D, H), D ** -0.5, 0.09375, ((0, 128),)),
        "w_down": centred(key_list[5], (EXPERTS, H, D), H ** -0.5, 0.1875, ((0, 128),)),
    }


def reference(tokens, expert_ids, gate_codes, w_gate, w_up, w_down):
    devices = N_GROUP * N_LOCAL
    block_ids = expert_ids.reshape(devices, TOK_DEV, TOPK)
    expert_range = jnp.arange(EXPERTS, dtype=jnp.int32)
    onehot = (block_ids[:, :, :, None] == expert_range[None, None, None, :]).astype(jnp.int32)
    present = jnp.sum(onehot, axis=2)
    before = jnp.cumsum(present, axis=1) - present
    slot_rank = jnp.sum(onehot * before[:, :, None, :], axis=3)
    kept = slot_rank < CAP
    device_index = jnp.arange(devices, dtype=jnp.int32)[:, None, None]
    total_slots = EXPERTS * devices * CAP
    slot_index = jnp.where(kept, block_ids * (devices * CAP) + device_index * CAP + slot_rank, total_slots).astype(jnp.int32)
    token_index = jnp.broadcast_to(device_index * TOK_DEV + jnp.arange(TOK_DEV, dtype=jnp.int32)[None, :, None], block_ids.shape).astype(jnp.int32)
    flat_index = slot_index.reshape(-1)
    slot_token = jnp.zeros((total_slots,), jnp.int32).at[flat_index].set(token_index.reshape(-1), mode="drop")
    slot_live = jnp.zeros((total_slots,), jnp.bool_).at[flat_index].set(True, mode="drop")

    def one_expert(operands):
        table, live, gate_mat, up_mat, down_mat = operands
        rows = jnp.where(live[:, None], tokens[table], jnp.zeros((), tokens.dtype))
        gate_part = jnp.dot(rows, gate_mat, preferred_element_type=jnp.float32)
        up_part = jnp.dot(rows, up_mat, preferred_element_type=jnp.float32)
        hidden = (jax.nn.silu(gate_part) * up_part).astype(jnp.bfloat16)
        result = jnp.dot(hidden, down_mat, preferred_element_type=jnp.float32).astype(jnp.bfloat16)
        return jnp.where(live[:, None], result, jnp.zeros((), jnp.bfloat16))

    expert_out = lax.map(one_expert, (slot_token.reshape(EXPERTS, devices * CAP), slot_live.reshape(EXPERTS, devices * CAP), w_gate, w_up, w_down))
    flat_out = expert_out.reshape(total_slots, D)
    picked = flat_out[jnp.minimum(flat_index, total_slots - 1)].reshape(TOKENS, TOPK, D)
    weight = jnp.where(kept.reshape(TOKENS, TOPK), gate_codes.astype(jnp.float32) / 1024.0, jnp.zeros((), jnp.float32))
    mixed = jnp.sum(weight[:, :, None] * picked.astype(jnp.float32), axis=1)
    return mixed.astype(jnp.bfloat16)
```

```python
import jax
import jax.numpy as jnp
from jax import lax
from jax.sharding import PartitionSpec as P


def expert_rows(rows, gate_mat, up_mat, down_mat):
    gate_part = jnp.dot(rows, gate_mat, preferred_element_type=jnp.float32)
    up_part = jnp.dot(rows, up_mat, preferred_element_type=jnp.float32)
    hidden = (jax.nn.silu(gate_part) * up_part).astype(jnp.bfloat16)
    return jnp.dot(hidden, down_mat, preferred_element_type=jnp.float32).astype(jnp.bfloat16)


def local(tokens, expert_ids, gate_codes, w_gate, w_up, w_down):
    tok_rows, width = tokens.shape
    top = expert_ids.shape[1]
    num_groups = lax.axis_size("group")
    num_local = lax.axis_size("local")
    experts = num_groups * num_local
    capacity = 2 * tok_rows * top // experts
    total_slots = experts * capacity
    expert_range = jnp.arange(experts, dtype=jnp.int32)
    onehot = (expert_ids[:, :, None] == expert_range[None, None, :]).astype(jnp.int32)
    present = jnp.sum(onehot, axis=1)
    before = jnp.cumsum(present, axis=0) - present
    slot_rank = jnp.sum(onehot * before[:, None, :], axis=2)
    kept = slot_rank < capacity
    slot_index = jnp.where(kept, slot_rank * experts + expert_ids, total_slots)
    slot_range = jnp.arange(total_slots, dtype=jnp.int32)
    route_hit = slot_index[:, :, None] == slot_range[None, None, :]
    pick = jnp.any(route_hit, axis=1)
    outgoing = jnp.dot(
        pick.T.astype(jnp.bfloat16), tokens, preferred_element_type=jnp.float32
    ).astype(jnp.bfloat16)
    got_rows = lax.all_to_all(
        outgoing.reshape(capacity, experts, width),
        ("group", "local"),
        split_axis=1,
        concat_axis=1,
        tiled=True,
    )
    rows_in = got_rows.reshape(total_slots, width)
    produced = expert_rows(rows_in, w_gate[0], w_up[0], w_down[0])
    returned = lax.all_to_all(
        produced.reshape(capacity, experts, width),
        ("group", "local"),
        split_axis=1,
        concat_axis=1,
        tiled=True,
    )
    back_flat = returned.reshape(total_slots, width)
    weight = jnp.where(kept, gate_codes.astype(jnp.float32) / 1024.0, jnp.zeros((), jnp.float32))
    combine = jnp.sum(jnp.where(route_hit, weight[:, :, None], 0.0), axis=1)
    combine_hi = combine.astype(jnp.bfloat16)
    combine_lo = (combine - combine_hi.astype(jnp.float32)).astype(jnp.bfloat16)
    mixed = jnp.dot(combine_hi, back_flat, preferred_element_type=jnp.float32) + jnp.dot(
        combine_lo, back_flat, preferred_element_type=jnp.float32
    )
    return mixed.astype(jnp.bfloat16)


def solution(mesh):
    placed = (
        P(("group", "local"), None),
        P(("group", "local"), None),
        P(("group", "local"), None),
        P(("group", "local"), None, None),
        P(("group", "local"), None, None),
        P(("group", "local"), None, None),
    )
    return jax.shard_map(
        local, mesh=mesh, in_specs=placed, out_specs=P(("group", "local"), None), check_vma=False
    )
```

```python
import jax
import jax.numpy as jnp
from jax import lax
from jax.experimental import pallas as pl
from jax.experimental.pallas import tpu as pltpu
from jax.sharding import PartitionSpec as P

H_BLOCK = 256


def mlp_kernel(x_ref, wg_ref, wu_ref, wd_ref, o_ref, acc_ref):
    j = pl.program_id(0)
    x = x_ref[...]
    gate_part = jnp.dot(x, wg_ref[...], preferred_element_type=jnp.float32)
    up_part = jnp.dot(x, wu_ref[...], preferred_element_type=jnp.float32)
    hidden = (gate_part / (1.0 + jnp.exp(-gate_part)) * up_part).astype(jnp.bfloat16)
    part = jnp.dot(hidden, wd_ref[...], preferred_element_type=jnp.float32)

    @pl.when(j == 0)
    def _():
        acc_ref[...] = part

    @pl.when(j > 0)
    def _():
        acc_ref[...] += part

    @pl.when(j == pl.num_programs(0) - 1)
    def _():
        o_ref[...] = acc_ref[...].astype(o_ref.dtype)


def expert_rows(rows, w_gate, w_up, w_down):
    slots, width = rows.shape
    hid = w_gate.shape[2]
    steps = hid // H_BLOCK
    cost = pl.CostEstimate(
        flops=6 * slots * width * hid,
        transcendentals=slots * hid,
        bytes_accessed=2 * (3 * width * hid + 2 * slots * width),
    )
    return pl.pallas_call(
        mlp_kernel,
        grid=(steps,),
        in_specs=[
            pl.BlockSpec((slots, width), lambda j: (0, 0)),
            pl.BlockSpec((None, width, H_BLOCK), lambda j: (0, 0, j)),
            pl.BlockSpec((None, width, H_BLOCK), lambda j: (0, 0, j)),
            pl.BlockSpec((None, H_BLOCK, width), lambda j: (0, j, 0)),
        ],
        out_specs=pl.BlockSpec((slots, width), lambda j: (0, 0)),
        out_shape=jax.ShapeDtypeStruct((slots, width), jnp.bfloat16),
        scratch_shapes=[pltpu.VMEM((slots, width), jnp.float32)],
        compiler_params=pltpu.CompilerParams(
            dimension_semantics=("arbitrary",), vmem_limit_bytes=48 * 1024 * 1024
        ),
        cost_estimate=cost,
    )(rows, w_gate, w_up, w_down)


def local(tokens, expert_ids, gate_codes, w_gate, w_up, w_down):
    tok_rows, width = tokens.shape
    top = expert_ids.shape[1]
    num_groups = lax.axis_size("group")
    num_local = lax.axis_size("local")
    experts = num_groups * num_local
    capacity = 2 * tok_rows * top // experts
    total_slots = experts * capacity
    expert_range = jnp.arange(experts, dtype=jnp.int32)
    onehot = (expert_ids[:, :, None] == expert_range[None, None, :]).astype(jnp.int32)
    present = jnp.sum(onehot, axis=1)
    before = jnp.cumsum(present, axis=0) - present
    slot_rank = jnp.sum(onehot * before[:, None, :], axis=2)
    kept = slot_rank < capacity
    slot_index = jnp.where(kept, slot_rank * experts + expert_ids, total_slots)
    slot_range = jnp.arange(total_slots, dtype=jnp.int32)
    route_hit = slot_index[:, :, None] == slot_range[None, None, :]
    pick = jnp.any(route_hit, axis=1)
    outgoing = jnp.dot(
        pick.T.astype(jnp.bfloat16), tokens, preferred_element_type=jnp.float32
    ).astype(jnp.bfloat16)
    got_rows = lax.all_to_all(
        outgoing.reshape(capacity, experts, width),
        ("group", "local"),
        split_axis=1,
        concat_axis=1,
        tiled=True,
    )
    rows_in = got_rows.reshape(total_slots, width)
    produced = expert_rows(rows_in, w_gate, w_up, w_down)
    returned = lax.all_to_all(
        produced.reshape(capacity, experts, width),
        ("group", "local"),
        split_axis=1,
        concat_axis=1,
        tiled=True,
    )
    back_flat = returned.reshape(total_slots, width)
    weight = jnp.where(kept, gate_codes.astype(jnp.float32) / 1024.0, jnp.zeros((), jnp.float32))
    combine = jnp.sum(jnp.where(route_hit, weight[:, :, None], 0.0), axis=1)
    combine_hi = lax.reduce_precision(combine, exponent_bits=8, mantissa_bits=7)
    combine_lo = combine - combine_hi
    mixed = jnp.dot(
        combine_hi.astype(jnp.bfloat16), back_flat, preferred_element_type=jnp.float32
    ) + jnp.dot(combine_lo.astype(jnp.bfloat16), back_flat, preferred_element_type=jnp.float32)
    return mixed.astype(jnp.bfloat16)


def solution(mesh):
    placed = (
        P(("group", "local"), None),
        P(("group", "local"), None),
        P(("group", "local"), None),
        P(("group", "local"), None, None),
        P(("group", "local"), None, None),
        P(("group", "local"), None, None),
    )
    return jax.shard_map(
        local, mesh=mesh, in_specs=placed, out_specs=P(("group", "local"), None), check_vma=False
    )
```

```python
import jax
import jax.numpy as jnp
from jax import lax
from jax.experimental import pallas as pl
from jax.experimental.pallas import tpu as pltpu
from jax.sharding import PartitionSpec as P

H_BLOCK = 256


def mlp_kernel(x_ref, wg_ref, wu_hbm, wd_hbm, o_ref, wu_buf, wd_buf, sems):
    steps = wg_ref.shape[2] // H_BLOCK

    def fetch(j):
        slot = j % 2
        cols = pl.ds(j * H_BLOCK, H_BLOCK)
        return (
            pltpu.make_async_copy(wu_hbm.at[0, :, cols], wu_buf.at[slot], sems.at[0, slot]),
            pltpu.make_async_copy(wd_hbm.at[0, cols, :], wd_buf.at[slot], sems.at[1, slot]),
        )

    x = x_ref[...]
    pending = fetch(0)
    for c in pending:
        c.start()
    acc = None
    for j in range(steps):
        slot = j % 2
        current = pending
        if j + 1 < steps:
            pending = fetch(j + 1)
            for c in pending:
                c.start()
        for c in current:
            c.wait()
        cols = pl.ds(j * H_BLOCK, H_BLOCK)
        gate_part = jnp.dot(x, wg_ref[0, :, cols], preferred_element_type=jnp.float32)
        up_part = jnp.dot(x, wu_buf[slot], preferred_element_type=jnp.float32)
        hidden = (gate_part / (1.0 + jnp.exp(-gate_part)) * up_part).astype(jnp.bfloat16)
        part = jnp.dot(hidden, wd_buf[slot], preferred_element_type=jnp.float32)
        acc = part if acc is None else acc + part
    o_ref[...] = acc.astype(o_ref.dtype)


def expert_rows(rows, w_gate, w_up, w_down):
    slots, width = rows.shape
    hid = w_gate.shape[2]
    cost = pl.CostEstimate(
        flops=6 * slots * width * hid,
        transcendentals=slots * hid,
        bytes_accessed=2 * (3 * width * hid + 2 * slots * width),
    )
    vmem = pl.BlockSpec(memory_space=pltpu.VMEM)
    anyspace = pl.BlockSpec(memory_space=pl.ANY)
    return pl.pallas_call(
        mlp_kernel,
        in_specs=[vmem, vmem, anyspace, anyspace],
        out_specs=vmem,
        out_shape=jax.ShapeDtypeStruct((slots, width), jnp.bfloat16),
        scratch_shapes=[
            pltpu.VMEM((2, width, H_BLOCK), jnp.bfloat16),
            pltpu.VMEM((2, H_BLOCK, width), jnp.bfloat16),
            pltpu.SemaphoreType.DMA((2, 2)),
        ],
        compiler_params=pltpu.CompilerParams(vmem_limit_bytes=40 * 1024 * 1024),
        cost_estimate=cost,
    )(rows, w_gate, w_up, w_down)


def local(tokens, expert_ids, gate_codes, w_gate, w_up, w_down):
    tok_rows, width = tokens.shape
    top = expert_ids.shape[1]
    num_groups = lax.axis_size("group")
    num_local = lax.axis_size("local")
    experts = num_groups * num_local
    capacity = 2 * tok_rows * top // experts
    total_slots = experts * capacity
    expert_range = jnp.arange(experts, dtype=jnp.int32)
    onehot = (expert_ids[:, :, None] == expert_range[None, None, :]).astype(jnp.int32)
    present = jnp.sum(onehot, axis=1)
    before = jnp.cumsum(present, axis=0) - present
    slot_rank = jnp.sum(onehot * before[:, None, :], axis=2)
    kept = slot_rank < capacity
    slot_index = jnp.where(kept, slot_rank * experts + expert_ids, total_slots)
    slot_range = jnp.arange(total_slots, dtype=jnp.int32)
    route_hit = slot_index[:, :, None] == slot_range[None, None, :]
    pick = jnp.any(route_hit, axis=1)
    outgoing = jnp.dot(
        pick.T.astype(jnp.bfloat16), tokens, preferred_element_type=jnp.float32
    ).astype(jnp.bfloat16)
    got_rows = lax.all_to_all(
        outgoing.reshape(capacity, experts, width),
        ("group", "local"),
        split_axis=1,
        concat_axis=1,
        tiled=True,
    )
    rows_in = got_rows.reshape(total_slots, width)
    produced = expert_rows(rows_in, w_gate, w_up, w_down)
    returned = lax.all_to_all(
        produced.reshape(capacity, experts, width),
        ("group", "local"),
        split_axis=1,
        concat_axis=1,
        tiled=True,
    )
    back_flat = returned.reshape(total_slots, width)
    weight = jnp.where(kept, gate_codes.astype(jnp.float32) / 1024.0, jnp.zeros((), jnp.float32))
    combine = jnp.sum(jnp.where(route_hit, weight[:, :, None], 0.0), axis=1)
    combine_hi = lax.reduce_precision(combine, exponent_bits=8, mantissa_bits=7)
    combine_lo = combine - combine_hi
    mixed = jnp.dot(
        combine_hi.astype(jnp.bfloat16), back_flat, preferred_element_type=jnp.float32
    ) + jnp.dot(combine_lo.astype(jnp.bfloat16), back_flat, preferred_element_type=jnp.float32)
    return mixed.astype(jnp.bfloat16)


def solution(mesh):
    placed = (
        P(("group", "local"), None),
        P(("group", "local"), None),
        P(("group", "local"), None),
        P(("group", "local"), None, None),
        P(("group", "local"), None, None),
        P(("group", "local"), None, None),
    )
    return jax.shard_map(
        local, mesh=mesh, in_specs=placed, out_specs=P(("group", "local"), None), check_vma=False
    )
```

```python
import jax
import jax.numpy as jnp
from jax import lax
from jax.experimental import pallas as pl
from jax.experimental.pallas import tpu as pltpu
from jax.sharding import PartitionSpec as P

H_BLOCK = 256


def mlp_kernel(x_ref, wg_ref, wu_hbm, wd_hbm, o_ref, wu_buf, wd_buf, sems):
    steps = wg_ref.shape[2] // H_BLOCK

    def fetch(j):
        slot = j % 2
        cols = pl.ds(j * H_BLOCK, H_BLOCK)
        return (
            pltpu.make_async_copy(wu_hbm.at[0, :, cols], wu_buf.at[slot], sems.at[0, slot]),
            pltpu.make_async_copy(wd_hbm.at[0, cols, :], wd_buf.at[slot], sems.at[1, slot]),
        )

    x = x_ref[...]
    pending = fetch(0)
    for c in pending:
        c.start()
    acc = None
    for j in range(steps):
        slot = j % 2
        current = pending
        if j + 1 < steps:
            pending = fetch(j + 1)
            for c in pending:
                c.start()
        for c in current:
            c.wait()
        cols = pl.ds(j * H_BLOCK, H_BLOCK)
        gate_part = jnp.dot(x, wg_ref[0, :, cols], preferred_element_type=jnp.float32)
        up_part = jnp.dot(x, wu_buf[slot], preferred_element_type=jnp.float32)
        hidden = (gate_part / (1.0 + jnp.exp(-gate_part)) * up_part).astype(jnp.bfloat16)
        part = jnp.dot(hidden, wd_buf[slot], preferred_element_type=jnp.float32)
        acc = part if acc is None else acc + part
    half = acc.shape[0] // 2
    for r in range(2):
        o_ref[:, r, :] = acc[r * half:(r + 1) * half].astype(o_ref.dtype)


def expert_rows(rows, w_gate, w_up, w_down):
    slots, width = rows.shape
    hid = w_gate.shape[2]
    cost = pl.CostEstimate(
        flops=6 * slots * width * hid,
        transcendentals=slots * hid,
        bytes_accessed=2 * (3 * width * hid + 2 * slots * width),
    )
    vmem = pl.BlockSpec(memory_space=pltpu.VMEM)
    anyspace = pl.BlockSpec(memory_space=pl.ANY)
    return pl.pallas_call(
        mlp_kernel,
        in_specs=[vmem, vmem, anyspace, anyspace],
        out_specs=vmem,
        out_shape=jax.ShapeDtypeStruct((slots // 2, 2, width), jnp.bfloat16),
        scratch_shapes=[
            pltpu.VMEM((2, width, H_BLOCK), jnp.bfloat16),
            pltpu.VMEM((2, H_BLOCK, width), jnp.bfloat16),
            pltpu.SemaphoreType.DMA((2, 2)),
        ],
        compiler_params=pltpu.CompilerParams(vmem_limit_bytes=40 * 1024 * 1024),
        cost_estimate=cost,
    )(rows, w_gate, w_up, w_down)


def local(tokens, expert_ids, gate_codes, w_gate, w_up, w_down):
    tok_rows, width = tokens.shape
    top = expert_ids.shape[1]
    num_groups = lax.axis_size("group")
    num_local = lax.axis_size("local")
    experts = num_groups * num_local
    capacity = 2 * tok_rows * top // experts
    total_slots = experts * capacity
    expert_range = jnp.arange(experts, dtype=jnp.int32)
    onehot = (expert_ids[:, :, None] == expert_range[None, None, :]).astype(jnp.int32)
    present = jnp.sum(onehot, axis=1)
    before = jnp.cumsum(present, axis=0) - present
    slot_rank = jnp.sum(onehot * before[:, None, :], axis=2)
    kept = slot_rank < capacity
    slot_index = jnp.where(kept, slot_rank * experts + expert_ids, total_slots)
    slot_range = jnp.arange(total_slots, dtype=jnp.int32)
    route_hit = slot_index[:, :, None] == slot_range[None, None, :]
    pick = jnp.any(route_hit, axis=1)
    outgoing = jnp.dot(
        pick.T.astype(jnp.bfloat16), tokens, preferred_element_type=jnp.float32
    ).astype(jnp.bfloat16)
    got_rows = lax.all_to_all(
        outgoing.reshape(capacity, experts, width),
        ("group", "local"),
        split_axis=1,
        concat_axis=1,
        tiled=True,
    )
    rows_in = got_rows.reshape(total_slots, width)
    produced = expert_rows(rows_in, w_gate, w_up, w_down)
    returned = lax.all_to_all(produced, ("group", "local"), split_axis=0, concat_axis=0, tiled=True)
    back_flat = jnp.swapaxes(returned, 0, 1).reshape(total_slots, width)
    weight = jnp.where(kept, gate_codes.astype(jnp.float32) / 1024.0, jnp.zeros((), jnp.float32))
    combine = jnp.sum(jnp.where(route_hit, weight[:, :, None], 0.0), axis=1)
    combine_hi = lax.reduce_precision(combine, exponent_bits=8, mantissa_bits=7)
    combine_lo = combine - combine_hi
    mixed = jnp.dot(
        combine_hi.astype(jnp.bfloat16), back_flat, preferred_element_type=jnp.float32
    ) + jnp.dot(combine_lo.astype(jnp.bfloat16), back_flat, preferred_element_type=jnp.float32)
    return mixed.astype(jnp.bfloat16)


def solution(mesh):
    placed = (
        P(("group", "local"), None),
        P(("group", "local"), None),
        P(("group", "local"), None),
        P(("group", "local"), None, None),
        P(("group", "local"), None, None),
        P(("group", "local"), None, None),
    )
    return jax.shard_map(
        local, mesh=mesh, in_specs=placed, out_specs=P(("group", "local"), None), check_vma=False
    )
```

```python
import jax
import jax.numpy as jnp
from jax import lax
from jax.experimental import pallas as pl
from jax.experimental.pallas import tpu as pltpu
from jax.sharding import PartitionSpec as P

H_BLOCK = 256


def mlp_kernel(x_ref, wg_ref, wu_hbm, wd_hbm, o_ref, wu_buf, wd_buf, sems):
    steps = wg_ref.shape[2] // H_BLOCK

    def fetch(j):
        slot = j % 2
        cols = pl.ds(j * H_BLOCK, H_BLOCK)
        return (
            pltpu.make_async_copy(wu_hbm.at[0, :, cols], wu_buf.at[slot], sems.at[0, slot]),
            pltpu.make_async_copy(wd_hbm.at[0, cols, :], wd_buf.at[slot], sems.at[1, slot]),
        )

    x = x_ref[...]
    pending = fetch(0)
    for c in pending:
        c.start()
    acc = None
    for j in range(steps):
        slot = j % 2
        current = pending
        if j + 1 < steps:
            pending = fetch(j + 1)
            for c in pending:
                c.start()
        for c in current:
            c.wait()
        cols = pl.ds(j * H_BLOCK, H_BLOCK)
        gate_part = jnp.dot(x, wg_ref[0, :, cols], preferred_element_type=jnp.float32)
        up_part = jnp.dot(x, wu_buf[slot], preferred_element_type=jnp.float32)
        hidden = (gate_part / (1.0 + jnp.exp(-gate_part)) * up_part).astype(jnp.bfloat16)
        part = jnp.dot(hidden, wd_buf[slot], preferred_element_type=jnp.float32)
        acc = part if acc is None else acc + part
    half = acc.shape[0] // 2
    for r in range(2):
        o_ref[:, r, :] = acc[r * half:(r + 1) * half].astype(o_ref.dtype)


def expert_rows(rows, w_gate, w_up, w_down):
    slots, width = rows.shape
    hid = w_gate.shape[2]
    cost = pl.CostEstimate(
        flops=6 * slots * width * hid,
        transcendentals=slots * hid,
        bytes_accessed=2 * (3 * width * hid + 2 * slots * width),
    )
    vmem = pl.BlockSpec(memory_space=pltpu.VMEM)
    anyspace = pl.BlockSpec(memory_space=pl.ANY)
    return pl.pallas_call(
        mlp_kernel,
        in_specs=[vmem, vmem, anyspace, anyspace],
        out_specs=vmem,
        out_shape=jax.ShapeDtypeStruct((slots // 2, 2, width), jnp.bfloat16),
        scratch_shapes=[
            pltpu.VMEM((2, width, H_BLOCK), jnp.bfloat16),
            pltpu.VMEM((2, H_BLOCK, width), jnp.bfloat16),
            pltpu.SemaphoreType.DMA((2, 2)),
        ],
        compiler_params=pltpu.CompilerParams(vmem_limit_bytes=40 * 1024 * 1024),
        cost_estimate=cost,
    )(rows, w_gate, w_up, w_down)


def build_kernel(pick_ref, tok_ref, o_ref):
    tokens = tok_ref[...]
    for r in range(o_ref.shape[1]):
        o_ref[:, r, :] = jnp.dot(
            pick_ref[r], tokens, preferred_element_type=jnp.float32
        ).astype(o_ref.dtype)


def build_rows(pick, tokens):
    ranks, experts, _ = pick.shape
    vmem = pl.BlockSpec(memory_space=pltpu.VMEM)
    return pl.pallas_call(
        build_kernel,
        in_specs=[vmem, vmem],
        out_specs=vmem,
        out_shape=jax.ShapeDtypeStruct((experts, ranks, tokens.shape[1]), tokens.dtype),
        compiler_params=pltpu.CompilerParams(vmem_limit_bytes=2 * 1024 * 1024),
    )(pick, tokens)


def local(tokens, expert_ids, gate_codes, w_gate, w_up, w_down):
    tok_rows, width = tokens.shape
    top = expert_ids.shape[1]
    num_groups = lax.axis_size("group")
    num_local = lax.axis_size("local")
    experts = num_groups * num_local
    capacity = 2 * tok_rows * top // experts
    total_slots = experts * capacity
    expert_range = jnp.arange(experts, dtype=jnp.int32)
    onehot = (expert_ids[:, :, None] == expert_range[None, None, :]).astype(jnp.int32)
    present = jnp.sum(onehot, axis=1)
    before = jnp.cumsum(present, axis=0) - present
    slot_rank = jnp.sum(onehot * before[:, None, :], axis=2)
    kept = slot_rank < capacity
    slot_index = jnp.where(kept, slot_rank * experts + expert_ids, total_slots)
    slot_range = jnp.arange(total_slots, dtype=jnp.int32)
    route_hit = slot_index[:, :, None] == slot_range[None, None, :]
    pick = jnp.any(route_hit, axis=1)
    outgoing = build_rows(pick.T.astype(jnp.bfloat16).reshape(capacity, experts, tok_rows), tokens)
    got_rows = lax.all_to_all(outgoing, ("group", "local"), split_axis=0, concat_axis=0, tiled=True)
    rows_in = jnp.swapaxes(got_rows, 0, 1).reshape(total_slots, width)
    produced = expert_rows(rows_in, w_gate, w_up, w_down)
    returned = lax.all_to_all(produced, ("group", "local"), split_axis=0, concat_axis=0, tiled=True)
    back_flat = jnp.swapaxes(returned, 0, 1).reshape(total_slots, width)
    weight = jnp.where(kept, gate_codes.astype(jnp.float32) / 1024.0, jnp.zeros((), jnp.float32))
    combine = jnp.sum(jnp.where(route_hit, weight[:, :, None], 0.0), axis=1)
    combine_hi = lax.reduce_precision(combine, exponent_bits=8, mantissa_bits=7)
    combine_lo = combine - combine_hi
    mixed = jnp.dot(
        combine_hi.astype(jnp.bfloat16), back_flat, preferred_element_type=jnp.float32
    ) + jnp.dot(combine_lo.astype(jnp.bfloat16), back_flat, preferred_element_type=jnp.float32)
    return mixed.astype(jnp.bfloat16)


def solution(mesh):
    placed = (
        P(("group", "local"), None),
        P(("group", "local"), None),
        P(("group", "local"), None),
        P(("group", "local"), None, None),
        P(("group", "local"), None, None),
        P(("group", "local"), None, None),
    )
    return jax.shard_map(
        local, mesh=mesh, in_specs=placed, out_specs=P(("group", "local"), None), check_vma=False
    )
```

```python
import jax
import jax.numpy as jnp
from jax import lax
from jax.experimental import pallas as pl
from jax.experimental.pallas import tpu as pltpu
from jax.sharding import PartitionSpec as P

H_BLOCK = 256


def mlp_kernel(x_ref, wg_ref, wu_hbm, wd_hbm, o_ref, wu_buf, wd_buf, sems):
    steps = wg_ref.shape[2] // H_BLOCK

    def fetch(j):
        slot = j % 2
        cols = pl.ds(j * H_BLOCK, H_BLOCK)
        return (
            pltpu.make_async_copy(wu_hbm.at[0, :, cols], wu_buf.at[slot], sems.at[0, slot]),
            pltpu.make_async_copy(wd_hbm.at[0, cols, :], wd_buf.at[slot], sems.at[1, slot]),
        )

    x = x_ref[...]
    pending = fetch(0)
    for c in pending:
        c.start()
    gate_all = jnp.dot(x, wg_ref[0], preferred_element_type=jnp.float32)
    acc = None
    for j in range(steps):
        slot = j % 2
        current = pending
        if j + 1 < steps:
            pending = fetch(j + 1)
            for c in pending:
                c.start()
        for c in current:
            c.wait()
        gate_part = gate_all[:, j * H_BLOCK:(j + 1) * H_BLOCK]
        up_part = jnp.dot(x, wu_buf[slot], preferred_element_type=jnp.float32)
        hidden = (gate_part / (1.0 + jnp.exp(-gate_part)) * up_part).astype(jnp.bfloat16)
        part = jnp.dot(hidden, wd_buf[slot], preferred_element_type=jnp.float32)
        acc = part if acc is None else acc + part
    half = acc.shape[0] // 2
    for r in range(2):
        o_ref[:, r, :] = acc[r * half:(r + 1) * half].astype(o_ref.dtype)


def expert_rows(rows, w_gate, w_up, w_down):
    slots, width = rows.shape
    hid = w_gate.shape[2]
    cost = pl.CostEstimate(
        flops=6 * slots * width * hid,
        transcendentals=slots * hid,
        bytes_accessed=2 * (3 * width * hid + 2 * slots * width),
    )
    vmem = pl.BlockSpec(memory_space=pltpu.VMEM)
    anyspace = pl.BlockSpec(memory_space=pl.ANY)
    return pl.pallas_call(
        mlp_kernel,
        in_specs=[vmem, vmem, anyspace, anyspace],
        out_specs=vmem,
        out_shape=jax.ShapeDtypeStruct((slots // 2, 2, width), jnp.bfloat16),
        scratch_shapes=[
            pltpu.VMEM((2, width, H_BLOCK), jnp.bfloat16),
            pltpu.VMEM((2, H_BLOCK, width), jnp.bfloat16),
            pltpu.SemaphoreType.DMA((2, 2)),
        ],
        compiler_params=pltpu.CompilerParams(vmem_limit_bytes=40 * 1024 * 1024),
        cost_estimate=cost,
    )(rows, w_gate, w_up, w_down)


def build_kernel(pick_ref, tok_ref, o_ref):
    tokens = tok_ref[...]
    for r in range(o_ref.shape[1]):
        o_ref[:, r, :] = jnp.dot(
            pick_ref[r], tokens, preferred_element_type=jnp.float32
        ).astype(o_ref.dtype)


def build_rows(pick, tokens):
    ranks, experts, _ = pick.shape
    vmem = pl.BlockSpec(memory_space=pltpu.VMEM)
    return pl.pallas_call(
        build_kernel,
        in_specs=[vmem, vmem],
        out_specs=vmem,
        out_shape=jax.ShapeDtypeStruct((experts, ranks, tokens.shape[1]), tokens.dtype),
        compiler_params=pltpu.CompilerParams(vmem_limit_bytes=2 * 1024 * 1024),
    )(pick, tokens)


def local(tokens, expert_ids, gate_codes, w_gate, w_up, w_down):
    tok_rows, width = tokens.shape
    top = expert_ids.shape[1]
    num_groups = lax.axis_size("group")
    num_local = lax.axis_size("local")
    experts = num_groups * num_local
    capacity = 2 * tok_rows * top // experts
    total_slots = experts * capacity
    expert_range = jnp.arange(experts, dtype=jnp.int32)
    onehot = (expert_ids[:, :, None] == expert_range[None, None, :]).astype(jnp.int32)
    present = jnp.sum(onehot, axis=1)
    before = jnp.cumsum(present, axis=0) - present
    slot_rank = jnp.sum(onehot * before[:, None, :], axis=2)
    kept = slot_rank < capacity
    slot_index = jnp.where(kept, slot_rank * experts + expert_ids, total_slots)
    slot_range = jnp.arange(total_slots, dtype=jnp.int32)
    route_hit = slot_index[:, :, None] == slot_range[None, None, :]
    pick = jnp.any(route_hit, axis=1)
    outgoing = build_rows(pick.T.astype(jnp.bfloat16).reshape(capacity, experts, tok_rows), tokens)
    got_rows = lax.all_to_all(outgoing, ("group", "local"), split_axis=0, concat_axis=0, tiled=True)
    rows_in = jnp.swapaxes(got_rows, 0, 1).reshape(total_slots, width)
    produced = expert_rows(rows_in, w_gate, w_up, w_down)
    returned = lax.all_to_all(produced, ("group", "local"), split_axis=0, concat_axis=0, tiled=True)
    back_flat = jnp.swapaxes(returned, 0, 1).reshape(total_slots, width)
    weight = jnp.where(kept, gate_codes.astype(jnp.float32) / 1024.0, jnp.zeros((), jnp.float32))
    combine = jnp.sum(jnp.where(route_hit, weight[:, :, None], 0.0), axis=1)
    combine_hi = lax.reduce_precision(combine, exponent_bits=8, mantissa_bits=7)
    combine_lo = combine - combine_hi
    mixed = jnp.dot(
        combine_hi.astype(jnp.bfloat16), back_flat, preferred_element_type=jnp.float32
    ) + jnp.dot(combine_lo.astype(jnp.bfloat16), back_flat, preferred_element_type=jnp.float32)
    return mixed.astype(jnp.bfloat16)


def solution(mesh):
    placed = (
        P(("group", "local"), None),
        P(("group", "local"), None),
        P(("group", "local"), None),
        P(("group", "local"), None, None),
        P(("group", "local"), None, None),
        P(("group", "local"), None, None),
    )
    return jax.shard_map(
        local, mesh=mesh, in_specs=placed, out_specs=P(("group", "local"), None), check_vma=False
    )
```

```python
import jax
import jax.numpy as jnp
from jax import lax
from jax.experimental import pallas as pl
from jax.experimental.pallas import tpu as pltpu
from jax.sharding import PartitionSpec as P

H_BLOCK = 256


def mlp_kernel(x_ref, wg_ref, wu_hbm, wd_hbm, o_ref, wu_buf, wd_all, hid_ref, sems):
    steps = wg_ref.shape[2] // H_BLOCK

    def fetch_up(j):
        cols = pl.ds(j * H_BLOCK, H_BLOCK)
        return pltpu.make_async_copy(wu_hbm.at[0, :, cols], wu_buf.at[j % 2], sems.at[0, j % 2])

    def fetch_down(j):
        rows = pl.ds(j * H_BLOCK, H_BLOCK)
        return pltpu.make_async_copy(wd_hbm.at[0, rows, :], wd_all.at[rows, :], sems.at[1, j])

    x = x_ref[...]
    up_next = fetch_up(0)
    up_next.start()
    downs = []
    for j in range(steps):
        up_now = up_next
        if j + 1 < steps:
            up_next = fetch_up(j + 1)
            up_next.start()
        downs.append(fetch_down(j))
        downs[-1].start()
        up_now.wait()
        cols = pl.ds(j * H_BLOCK, H_BLOCK)
        gate_part = jnp.dot(x, wg_ref[0, :, cols], preferred_element_type=jnp.float32)
        up_part = jnp.dot(x, wu_buf[j % 2], preferred_element_type=jnp.float32)
        hid_ref[:, cols] = (gate_part / (1.0 + jnp.exp(-gate_part)) * up_part).astype(jnp.bfloat16)
    for c in downs:
        c.wait()
    acc = jnp.dot(hid_ref[...], wd_all[...], preferred_element_type=jnp.float32)
    half = acc.shape[0] // 2
    for r in range(2):
        o_ref[:, r, :] = acc[r * half:(r + 1) * half].astype(o_ref.dtype)


def expert_rows(rows, w_gate, w_up, w_down):
    slots, width = rows.shape
    hid = w_gate.shape[2]
    cost = pl.CostEstimate(
        flops=6 * slots * width * hid,
        transcendentals=slots * hid,
        bytes_accessed=2 * (3 * width * hid + 2 * slots * width),
    )
    vmem = pl.BlockSpec(memory_space=pltpu.VMEM)
    anyspace = pl.BlockSpec(memory_space=pl.ANY)
    return pl.pallas_call(
        mlp_kernel,
        in_specs=[vmem, vmem, anyspace, anyspace],
        out_specs=vmem,
        out_shape=jax.ShapeDtypeStruct((slots // 2, 2, width), jnp.bfloat16),
        scratch_shapes=[
            pltpu.VMEM((2, width, H_BLOCK), jnp.bfloat16),
            pltpu.VMEM((hid, width), jnp.bfloat16),
            pltpu.VMEM((slots, hid), jnp.bfloat16),
            pltpu.SemaphoreType.DMA((2, hid // H_BLOCK)),
        ],
        compiler_params=pltpu.CompilerParams(vmem_limit_bytes=40 * 1024 * 1024),
        cost_estimate=cost,
    )(rows, w_gate, w_up, w_down)


def build_kernel(pick_ref, tok_ref, o_ref):
    tokens = tok_ref[...]
    for r in range(o_ref.shape[1]):
        o_ref[:, r, :] = jnp.dot(
            pick_ref[r], tokens, preferred_element_type=jnp.float32
        ).astype(o_ref.dtype)


def build_rows(pick, tokens):
    ranks, experts, _ = pick.shape
    vmem = pl.BlockSpec(memory_space=pltpu.VMEM)
    return pl.pallas_call(
        build_kernel,
        in_specs=[vmem, vmem],
        out_specs=vmem,
        out_shape=jax.ShapeDtypeStruct((experts, ranks, tokens.shape[1]), tokens.dtype),
        compiler_params=pltpu.CompilerParams(vmem_limit_bytes=2 * 1024 * 1024),
    )(pick, tokens)


def local(tokens, expert_ids, gate_codes, w_gate, w_up, w_down):
    tok_rows, width = tokens.shape
    top = expert_ids.shape[1]
    num_groups = lax.axis_size("group")
    num_local = lax.axis_size("local")
    experts = num_groups * num_local
    capacity = 2 * tok_rows * top // experts
    total_slots = experts * capacity
    expert_range = jnp.arange(experts, dtype=jnp.int32)
    onehot = (expert_ids[:, :, None] == expert_range[None, None, :]).astype(jnp.int32)
    present = jnp.sum(onehot, axis=1)
    before = jnp.cumsum(present, axis=0) - present
    slot_rank = jnp.sum(onehot * before[:, None, :], axis=2)
    kept = slot_rank < capacity
    slot_index = jnp.where(kept, slot_rank * experts + expert_ids, total_slots)
    slot_range = jnp.arange(total_slots, dtype=jnp.int32)
    route_hit = slot_index[:, :, None] == slot_range[None, None, :]
    pick = jnp.any(route_hit, axis=1)
    outgoing = build_rows(pick.T.astype(jnp.bfloat16).reshape(capacity, experts, tok_rows), tokens)
    got_rows = lax.all_to_all(outgoing, ("group", "local"), split_axis=0, concat_axis=0, tiled=True)
    rows_in = jnp.swapaxes(got_rows, 0, 1).reshape(total_slots, width)
    produced = expert_rows(rows_in, w_gate, w_up, w_down)
    returned = lax.all_to_all(produced, ("group", "local"), split_axis=0, concat_axis=0, tiled=True)
    back_flat = jnp.swapaxes(returned, 0, 1).reshape(total_slots, width)
    weight = jnp.where(kept, gate_codes.astype(jnp.float32) / 1024.0, jnp.zeros((), jnp.float32))
    combine = jnp.sum(jnp.where(route_hit, weight[:, :, None], 0.0), axis=1)
    combine_hi = lax.reduce_precision(combine, exponent_bits=8, mantissa_bits=7)
    combine_lo = combine - combine_hi
    mixed = jnp.dot(
        combine_hi.astype(jnp.bfloat16), back_flat, preferred_element_type=jnp.float32
    ) + jnp.dot(combine_lo.astype(jnp.bfloat16), back_flat, preferred_element_type=jnp.float32)
    return mixed.astype(jnp.bfloat16)


def solution(mesh):
    placed = (
        P(("group", "local"), None),
        P(("group", "local"), None),
        P(("group", "local"), None),
        P(("group", "local"), None, None),
        P(("group", "local"), None, None),
        P(("group", "local"), None, None),
    )
    return jax.shard_map(
        local, mesh=mesh, in_specs=placed, out_specs=P(("group", "local"), None), check_vma=False
    )
```

```python
import jax
import jax.numpy as jnp
from jax import lax
from jax.experimental import pallas as pl
from jax.experimental.pallas import tpu as pltpu
from jax.sharding import PartitionSpec as P

H_BLOCK = 256


def mlp_kernel(x_ref, wg_ref, wu_hbm, wd_hbm, o_ref, wu_buf, wd_all, hid_ref, sems):
    steps = wg_ref.shape[2] // H_BLOCK

    def fetch_up(j):
        cols = pl.ds(j * H_BLOCK, H_BLOCK)
        return pltpu.make_async_copy(wu_hbm.at[0, :, cols], wu_buf.at[j % 2], sems.at[0, j % 2])

    def fetch_down(j):
        rows = pl.ds(j * H_BLOCK, H_BLOCK)
        return pltpu.make_async_copy(wd_hbm.at[0, rows, :], wd_all.at[rows, :], sems.at[1, j])

    x = x_ref[...]
    up_next = fetch_up(0)
    up_next.start()
    downs = []
    for j in range(steps):
        up_now = up_next
        if j + 1 < steps:
            up_next = fetch_up(j + 1)
            up_next.start()
        downs.append(fetch_down(j))
        downs[-1].start()
        up_now.wait()
        cols = pl.ds(j * H_BLOCK, H_BLOCK)
        gate_part = jnp.dot(x, wg_ref[0, :, cols], preferred_element_type=jnp.float32)
        up_part = jnp.dot(x, wu_buf[j % 2], preferred_element_type=jnp.float32)
        hid_ref[:, cols] = (gate_part / (1.0 + jnp.exp(-gate_part)) * up_part).astype(jnp.bfloat16)
    for c in downs:
        c.wait()
    acc = jnp.dot(hid_ref[...], wd_all[...], preferred_element_type=jnp.float32)
    half = acc.shape[0] // 2
    for r in range(2):
        o_ref[:, r, :] = acc[r * half:(r + 1) * half].astype(o_ref.dtype)


def expert_rows(rows, w_gate, w_up, w_down):
    slots, width = rows.shape
    hid = w_gate.shape[2]
    cost = pl.CostEstimate(
        flops=6 * slots * width * hid,
        transcendentals=slots * hid,
        bytes_accessed=2 * (3 * width * hid + 2 * slots * width),
    )
    vmem = pl.BlockSpec(memory_space=pltpu.VMEM)
    anyspace = pl.BlockSpec(memory_space=pl.ANY)
    return pl.pallas_call(
        mlp_kernel,
        in_specs=[vmem, vmem, anyspace, anyspace],
        out_specs=vmem,
        out_shape=jax.ShapeDtypeStruct((slots // 2, 2, width), jnp.bfloat16),
        scratch_shapes=[
            pltpu.VMEM((2, width, H_BLOCK), jnp.bfloat16),
            pltpu.VMEM((hid, width), jnp.bfloat16),
            pltpu.VMEM((slots, hid), jnp.bfloat16),
            pltpu.SemaphoreType.DMA((2, hid // H_BLOCK)),
        ],
        compiler_params=pltpu.CompilerParams(vmem_limit_bytes=40 * 1024 * 1024),
        cost_estimate=cost,
    )(rows, w_gate, w_up, w_down)


def build_kernel(pick_ref, tok_ref, o_ref):
    tokens = tok_ref[...]
    for r in range(o_ref.shape[1]):
        o_ref[:, r, :] = jnp.dot(
            pick_ref[r], tokens, preferred_element_type=jnp.float32
        ).astype(o_ref.dtype)


def build_rows(pick, tokens):
    ranks, experts, _ = pick.shape
    vmem = pl.BlockSpec(memory_space=pltpu.VMEM)
    return pl.pallas_call(
        build_kernel,
        in_specs=[vmem, vmem],
        out_specs=vmem,
        out_shape=jax.ShapeDtypeStruct((experts, ranks, tokens.shape[1]), tokens.dtype),
        compiler_params=pltpu.CompilerParams(vmem_limit_bytes=2 * 1024 * 1024),
    )(pick, tokens)


def local(tokens, expert_ids, gate_codes, w_gate, w_up, w_down):
    tok_rows, width = tokens.shape
    top = expert_ids.shape[1]
    num_groups = lax.axis_size("group")
    num_local = lax.axis_size("local")
    experts = num_groups * num_local
    capacity = 2 * tok_rows * top // experts
    total_slots = experts * capacity
    expert_range = jnp.arange(experts, dtype=jnp.int32)
    onehot = (expert_ids[:, :, None] == expert_range[None, None, :]).astype(jnp.int32)
    present = jnp.sum(onehot, axis=1)
    before = jnp.cumsum(present, axis=0) - present
    slot_rank = jnp.sum(onehot * before[:, None, :], axis=2)
    kept = slot_rank < capacity
    slot_index = jnp.where(kept, slot_rank * experts + expert_ids, total_slots)
    slot_range = jnp.arange(total_slots, dtype=jnp.int32)
    route_hit = slot_index[:, :, None] == slot_range[None, None, :]
    pick = jnp.any(route_hit, axis=1)
    outgoing = build_rows(pick.T.astype(jnp.bfloat16).reshape(capacity, experts, tok_rows), tokens)
    got_rows = lax.all_to_all(outgoing, ("group", "local"), split_axis=0, concat_axis=0, tiled=True)
    rows_in = jnp.swapaxes(got_rows, 0, 1).reshape(total_slots, width)
    produced = expert_rows(rows_in, w_gate, w_up, w_down)
    returned = lax.all_to_all(produced, ("group", "local"), split_axis=0, concat_axis=0, tiled=True)
    back_flat = jnp.swapaxes(returned, 0, 1).reshape(total_slots, width)
    weight = jnp.where(kept, gate_codes.astype(jnp.float32) / 1024.0, jnp.zeros((), jnp.float32))
    combine = jnp.sum(jnp.where(route_hit, weight[:, :, None], 0.0), axis=1)
    combine_hi = lax.reduce_precision(combine, exponent_bits=8, mantissa_bits=7)
    combine_lo = combine - combine_hi
    split = jnp.concatenate([combine_hi, combine_lo], axis=0).astype(jnp.bfloat16)
    both = jnp.dot(split, back_flat, preferred_element_type=jnp.float32)
    mixed = both[:tok_rows] + both[tok_rows:]
    return mixed.astype(jnp.bfloat16)


def solution(mesh):
    placed = (
        P(("group", "local"), None),
        P(("group", "local"), None),
        P(("group", "local"), None),
        P(("group", "local"), None, None),
        P(("group", "local"), None, None),
        P(("group", "local"), None, None),
    )
    return jax.shard_map(
        local, mesh=mesh, in_specs=placed, out_specs=P(("group", "local"), None), check_vma=False
    )
```

```python
import jax
import jax.numpy as jnp
from jax import lax
from jax.experimental import pallas as pl
from jax.experimental.pallas import tpu as pltpu
from jax.sharding import PartitionSpec as P

H_BLOCK = 256


def mlp_kernel(x_ref, wg_ref, wu_hbm, wd_hbm, o_ref, wu_buf, wd_all, hid_ref, sems):
    steps = wg_ref.shape[2] // H_BLOCK

    def fetch_up(j):
        cols = pl.ds(j * H_BLOCK, H_BLOCK)
        return pltpu.make_async_copy(wu_hbm.at[0, :, cols], wu_buf.at[j % 2], sems.at[0, j % 2])

    def fetch_down(j):
        rows = pl.ds(j * H_BLOCK, H_BLOCK)
        return pltpu.make_async_copy(wd_hbm.at[0, rows, :], wd_all.at[rows, :], sems.at[1, j])

    x = x_ref[...]
    up_next = fetch_up(0)
    up_next.start()
    downs = []
    for j in range(steps):
        up_now = up_next
        if j + 1 < steps:
            up_next = fetch_up(j + 1)
            up_next.start()
        downs.append(fetch_down(j))
        downs[-1].start()
        up_now.wait()
        cols = pl.ds(j * H_BLOCK, H_BLOCK)
        gate_part = jnp.dot(x, wg_ref[0, :, cols], preferred_element_type=jnp.float32)
        up_part = jnp.dot(x, wu_buf[j % 2], preferred_element_type=jnp.float32)
        hid_ref[:, cols] = (gate_part / (1.0 + jnp.exp(-gate_part)) * up_part).astype(jnp.bfloat16)
    for c in downs:
        c.wait()
    acc = jnp.dot(hid_ref[...], wd_all[...], preferred_element_type=jnp.float32)
    half = acc.shape[0] // 2
    for r in range(2):
        o_ref[:, r, :] = acc[r * half:(r + 1) * half].astype(o_ref.dtype)


def expert_rows(rows, w_gate, w_up, w_down):
    slots, width = rows.shape
    hid = w_gate.shape[2]
    cost = pl.CostEstimate(
        flops=6 * slots * width * hid,
        transcendentals=slots * hid,
        bytes_accessed=2 * (3 * width * hid + 2 * slots * width),
    )
    vmem = pl.BlockSpec(memory_space=pltpu.VMEM)
    anyspace = pl.BlockSpec(memory_space=pl.ANY)
    return pl.pallas_call(
        mlp_kernel,
        in_specs=[vmem, vmem, anyspace, anyspace],
        out_specs=vmem,
        out_shape=jax.ShapeDtypeStruct((slots // 2, 2, width), jnp.bfloat16),
        scratch_shapes=[
            pltpu.VMEM((2, width, H_BLOCK), jnp.bfloat16),
            pltpu.VMEM((hid, width), jnp.bfloat16),
            pltpu.VMEM((slots, hid), jnp.bfloat16),
            pltpu.SemaphoreType.DMA((2, hid // H_BLOCK)),
        ],
        compiler_params=pltpu.CompilerParams(vmem_limit_bytes=40 * 1024 * 1024),
        cost_estimate=cost,
    )(rows, w_gate, w_up, w_down)


def build_kernel(ids_ref, tok_hbm, o_ref, tok_buf, sem):
    copy = pltpu.make_async_copy(tok_hbm, tok_buf, sem)
    copy.start()
    top, tok_rows = ids_ref.shape
    experts, ranks, _ = o_ref.shape
    ids = ids_ref[...]
    expert_col = lax.broadcasted_iota(jnp.int32, (experts, tok_rows), 0)
    present = ids[0:1, :] == expert_col
    for k in range(1, top):
        present = present | (ids[k:k + 1, :] == expert_col)
    earlier = lax.broadcasted_iota(jnp.int32, (tok_rows, tok_rows), 0) < lax.broadcasted_iota(
        jnp.int32, (tok_rows, tok_rows), 1
    )
    before = jnp.dot(
        present.astype(jnp.float32), earlier.astype(jnp.float32), preferred_element_type=jnp.float32
    )
    copy.wait()
    tokens = tok_buf[...]
    for r in range(ranks):
        pick = jnp.where(present & (before == r), 1.0, 0.0).astype(tokens.dtype)
        o_ref[:, r, :] = jnp.dot(pick, tokens, preferred_element_type=jnp.float32).astype(o_ref.dtype)


def build_rows(ids_t, tokens, experts, ranks):
    vmem = pl.BlockSpec(memory_space=pltpu.VMEM)
    return pl.pallas_call(
        build_kernel,
        in_specs=[vmem, pl.BlockSpec(memory_space=pl.ANY)],
        out_specs=vmem,
        out_shape=jax.ShapeDtypeStruct((experts, ranks, tokens.shape[1]), tokens.dtype),
        scratch_shapes=[pltpu.VMEM(tokens.shape, tokens.dtype), pltpu.SemaphoreType.DMA(())],
        compiler_params=pltpu.CompilerParams(vmem_limit_bytes=2 * 1024 * 1024),
    )(ids_t, tokens)


def local(tokens, expert_ids, gate_codes, w_gate, w_up, w_down):
    tok_rows, width = tokens.shape
    top = expert_ids.shape[1]
    num_groups = lax.axis_size("group")
    num_local = lax.axis_size("local")
    experts = num_groups * num_local
    capacity = 2 * tok_rows * top // experts
    total_slots = experts * capacity
    outgoing = build_rows(expert_ids.T, tokens, experts, capacity)
    got_rows = lax.all_to_all(outgoing, ("group", "local"), split_axis=0, concat_axis=0, tiled=True)
    expert_ids, got_rows = lax.optimization_barrier((expert_ids, got_rows))
    rows_in = jnp.swapaxes(got_rows, 0, 1).reshape(total_slots, width)
    expert_range = jnp.arange(experts, dtype=jnp.int32)
    onehot = (expert_ids[:, :, None] == expert_range[None, None, :]).astype(jnp.int32)
    present = jnp.sum(onehot, axis=1)
    before = jnp.cumsum(present, axis=0) - present
    slot_rank = jnp.sum(onehot * before[:, None, :], axis=2)
    kept = slot_rank < capacity
    slot_index = jnp.where(kept, slot_rank * experts + expert_ids, total_slots)
    slot_range = jnp.arange(total_slots, dtype=jnp.int32)
    route_hit = slot_index[:, :, None] == slot_range[None, None, :]
    produced = expert_rows(rows_in, w_gate, w_up, w_down)
    returned = lax.all_to_all(produced, ("group", "local"), split_axis=0, concat_axis=0, tiled=True)
    back_flat = jnp.swapaxes(returned, 0, 1).reshape(total_slots, width)
    weight = jnp.where(kept, gate_codes.astype(jnp.float32) / 1024.0, jnp.zeros((), jnp.float32))
    combine = jnp.sum(jnp.where(route_hit, weight[:, :, None], 0.0), axis=1)
    combine_hi = lax.reduce_precision(combine, exponent_bits=8, mantissa_bits=7)
    combine_lo = combine - combine_hi
    split = jnp.concatenate([combine_hi, combine_lo], axis=0).astype(jnp.bfloat16)
    both = jnp.dot(split, back_flat, preferred_element_type=jnp.float32)
    mixed = both[:tok_rows] + both[tok_rows:]
    return mixed.astype(jnp.bfloat16)


def solution(mesh):
    placed = (
        P(("group", "local"), None),
        P(("group", "local"), None),
        P(("group", "local"), None),
        P(("group", "local"), None, None),
        P(("group", "local"), None, None),
        P(("group", "local"), None, None),
    )
    return jax.shard_map(
        local, mesh=mesh, in_specs=placed, out_specs=P(("group", "local"), None), check_vma=False
    )
```

```python
import jax
import jax.numpy as jnp
from jax import lax
from jax.experimental import pallas as pl
from jax.experimental.pallas import tpu as pltpu
from jax.sharding import PartitionSpec as P

H_BLOCK = 256


def mlp_kernel(x_ref, wg_ref, wu_hbm, wd_hbm, o_ref, wu_buf, wd_all, hid_ref, sems):
    steps = wg_ref.shape[2] // H_BLOCK

    def fetch_up(j):
        cols = pl.ds(j * H_BLOCK, H_BLOCK)
        return pltpu.make_async_copy(wu_hbm.at[0, :, cols], wu_buf.at[j % 2], sems.at[0, j % 2])

    def fetch_down(j):
        rows = pl.ds(j * H_BLOCK, H_BLOCK)
        return pltpu.make_async_copy(wd_hbm.at[0, rows, :], wd_all.at[rows, :], sems.at[1, j])

    x = x_ref[...]
    up_next = fetch_up(0)
    up_next.start()
    downs = []
    for j in range(steps):
        up_now = up_next
        if j + 1 < steps:
            up_next = fetch_up(j + 1)
            up_next.start()
        downs.append(fetch_down(j))
        downs[-1].start()
        up_now.wait()
        cols = pl.ds(j * H_BLOCK, H_BLOCK)
        gate_part = jnp.dot(x, wg_ref[0, :, cols], preferred_element_type=jnp.float32)
        up_part = jnp.dot(x, wu_buf[j % 2], preferred_element_type=jnp.float32)
        hid_ref[:, cols] = (gate_part / (1.0 + jnp.exp(-gate_part)) * up_part).astype(jnp.bfloat16)
    for c in downs:
        c.wait()
    acc = jnp.dot(hid_ref[...], wd_all[...], preferred_element_type=jnp.float32)
    half = acc.shape[0] // 2
    for r in range(2):
        o_ref[:, r, :] = acc[r * half:(r + 1) * half].astype(o_ref.dtype)


def expert_rows(rows, w_gate, w_up, w_down):
    slots, width = rows.shape
    hid = w_gate.shape[2]
    cost = pl.CostEstimate(
        flops=6 * slots * width * hid,
        transcendentals=slots * hid,
        bytes_accessed=2 * (3 * width * hid + 2 * slots * width),
    )
    vmem = pl.BlockSpec(memory_space=pltpu.VMEM)
    anyspace = pl.BlockSpec(memory_space=pl.ANY)
    return pl.pallas_call(
        mlp_kernel,
        in_specs=[vmem, vmem, anyspace, anyspace],
        out_specs=vmem,
        out_shape=jax.ShapeDtypeStruct((slots // 2, 2, width), jnp.bfloat16),
        scratch_shapes=[
            pltpu.VMEM((2, width, H_BLOCK), jnp.bfloat16),
            pltpu.VMEM((hid, width), jnp.bfloat16),
            pltpu.VMEM((slots, hid), jnp.bfloat16),
            pltpu.SemaphoreType.DMA((2, hid // H_BLOCK)),
        ],
        compiler_params=pltpu.CompilerParams(vmem_limit_bytes=40 * 1024 * 1024),
        cost_estimate=cost,
    )(rows, w_gate, w_up, w_down)


def build_kernel(ids_hbm, tok_hbm, o_ref, ids_buf, tok_buf, sems):
    copy = pltpu.make_async_copy(tok_hbm, tok_buf, sems.at[0])
    copy.start()
    ids_copy = pltpu.make_async_copy(ids_hbm, ids_buf, sems.at[1])
    ids_copy.start()
    top, tok_rows = ids_buf.shape
    experts, ranks, _ = o_ref.shape
    ids_copy.wait()
    ids = ids_buf[...]
    expert_col = lax.broadcasted_iota(jnp.int32, (experts, tok_rows), 0)
    present = ids[0:1, :] == expert_col
    for k in range(1, top):
        present = present | (ids[k:k + 1, :] == expert_col)
    earlier = lax.broadcasted_iota(jnp.int32, (tok_rows, tok_rows), 0) < lax.broadcasted_iota(
        jnp.int32, (tok_rows, tok_rows), 1
    )
    before = jnp.dot(
        present.astype(jnp.float32), earlier.astype(jnp.float32), preferred_element_type=jnp.float32
    )
    copy.wait()
    tokens = tok_buf[...]
    for r in range(ranks):
        pick = jnp.where(present & (before == r), 1.0, 0.0).astype(tokens.dtype)
        o_ref[:, r, :] = jnp.dot(pick, tokens, preferred_element_type=jnp.float32).astype(o_ref.dtype)


def build_rows(ids_t, tokens, experts, ranks):
    vmem = pl.BlockSpec(memory_space=pltpu.VMEM)
    return pl.pallas_call(
        build_kernel,
        in_specs=[pl.BlockSpec(memory_space=pl.ANY), pl.BlockSpec(memory_space=pl.ANY)],
        out_specs=vmem,
        out_shape=jax.ShapeDtypeStruct((experts, ranks, tokens.shape[1]), tokens.dtype),
        scratch_shapes=[
            pltpu.VMEM(ids_t.shape, ids_t.dtype),
            pltpu.VMEM(tokens.shape, tokens.dtype),
            pltpu.SemaphoreType.DMA((2,)),
        ],
        compiler_params=pltpu.CompilerParams(vmem_limit_bytes=56 * 1024 * 1024),
    )(ids_t, tokens)


def local(tokens, expert_ids, gate_codes, w_gate, w_up, w_down):
    tok_rows, width = tokens.shape
    top = expert_ids.shape[1]
    num_groups = lax.axis_size("group")
    num_local = lax.axis_size("local")
    experts = num_groups * num_local
    capacity = 2 * tok_rows * top // experts
    total_slots = experts * capacity
    outgoing = build_rows(expert_ids.T, tokens, experts, capacity)
    got_rows = lax.all_to_all(outgoing, ("group", "local"), split_axis=0, concat_axis=0, tiled=True)
    expert_ids, got_rows = lax.optimization_barrier((expert_ids, got_rows))
    rows_in = jnp.swapaxes(got_rows, 0, 1).reshape(total_slots, width)
    expert_range = jnp.arange(experts, dtype=jnp.int32)
    onehot = (expert_ids[:, :, None] == expert_range[None, None, :]).astype(jnp.int32)
    present = jnp.sum(onehot, axis=1)
    before = jnp.cumsum(present, axis=0) - present
    slot_rank = jnp.sum(onehot * before[:, None, :], axis=2)
    kept = slot_rank < capacity
    slot_index = jnp.where(kept, slot_rank * experts + expert_ids, total_slots)
    slot_range = jnp.arange(total_slots, dtype=jnp.int32)
    route_hit = slot_index[:, :, None] == slot_range[None, None, :]
    produced = expert_rows(rows_in, w_gate, w_up, w_down)
    returned = lax.all_to_all(produced, ("group", "local"), split_axis=0, concat_axis=0, tiled=True)
    back_flat = jnp.swapaxes(returned, 0, 1).reshape(total_slots, width)
    weight = jnp.where(kept, gate_codes.astype(jnp.float32) / 1024.0, jnp.zeros((), jnp.float32))
    combine = jnp.sum(jnp.where(route_hit, weight[:, :, None], 0.0), axis=1)
    combine_hi = lax.reduce_precision(combine, exponent_bits=8, mantissa_bits=7)
    combine_lo = combine - combine_hi
    split = jnp.concatenate([combine_hi, combine_lo], axis=0).astype(jnp.bfloat16)
    both = jnp.dot(split, back_flat, preferred_element_type=jnp.float32)
    mixed = both[:tok_rows] + both[tok_rows:]
    return mixed.astype(jnp.bfloat16)


def solution(mesh):
    placed = (
        P(("group", "local"), None),
        P(("group", "local"), None),
        P(("group", "local"), None),
        P(("group", "local"), None, None),
        P(("group", "local"), None, None),
        P(("group", "local"), None, None),
    )
    return jax.shard_map(
        local, mesh=mesh, in_specs=placed, out_specs=P(("group", "local"), None), check_vma=False
    )
```

```python
import jax
import jax.numpy as jnp
from jax import lax
from jax.experimental import pallas as pl
from jax.experimental.pallas import tpu as pltpu
from jax.sharding import PartitionSpec as P

H_BLOCK = 256


def mlp_kernel(x_ref, wg_ref, wu_hbm, wd_hbm, o_ref, wu_buf, wd_all, hid_ref, sems):
    steps = wg_ref.shape[2] // H_BLOCK

    def fetch_up(j):
        cols = pl.ds(j * H_BLOCK, H_BLOCK)
        return pltpu.make_async_copy(wu_hbm.at[0, :, cols], wu_buf.at[j % 2], sems.at[0, j % 2])

    def fetch_down(j):
        rows = pl.ds(j * H_BLOCK, H_BLOCK)
        return pltpu.make_async_copy(wd_hbm.at[0, rows, :], wd_all.at[rows, :], sems.at[1, j])

    x = x_ref[...]
    up_next = fetch_up(0)
    up_next.start()
    downs = []
    for j in range(steps):
        up_now = up_next
        if j + 1 < steps:
            up_next = fetch_up(j + 1)
            up_next.start()
        downs.append(fetch_down(j))
        downs[-1].start()
        up_now.wait()
        cols = pl.ds(j * H_BLOCK, H_BLOCK)
        gate_part = jnp.dot(x, wg_ref[0, :, cols], preferred_element_type=jnp.float32)
        up_part = jnp.dot(x, wu_buf[j % 2], preferred_element_type=jnp.float32)
        hid_ref[:, cols] = (gate_part / (1.0 + jnp.exp(-gate_part)) * up_part).astype(jnp.bfloat16)
    for c in downs:
        c.wait()
    acc = jnp.dot(hid_ref[...], wd_all[...], preferred_element_type=jnp.float32)
    half = acc.shape[0] // 2
    for r in range(2):
        o_ref[:, r, :] = acc[r * half:(r + 1) * half].astype(o_ref.dtype)


def expert_rows(rows, w_gate, w_up, w_down):
    slots, width = rows.shape
    hid = w_gate.shape[2]
    cost = pl.CostEstimate(
        flops=6 * slots * width * hid,
        transcendentals=slots * hid,
        bytes_accessed=2 * (3 * width * hid + 2 * slots * width),
    )
    vmem = pl.BlockSpec(memory_space=pltpu.VMEM)
    anyspace = pl.BlockSpec(memory_space=pl.ANY)
    return pl.pallas_call(
        mlp_kernel,
        in_specs=[vmem, vmem, anyspace, anyspace],
        out_specs=vmem,
        out_shape=jax.ShapeDtypeStruct((slots // 2, 2, width), jnp.bfloat16),
        scratch_shapes=[
            pltpu.VMEM((2, width, H_BLOCK), jnp.bfloat16),
            pltpu.VMEM((hid, width), jnp.bfloat16),
            pltpu.VMEM((slots, hid), jnp.bfloat16),
            pltpu.SemaphoreType.DMA((2, hid // H_BLOCK)),
        ],
        compiler_params=pltpu.CompilerParams(vmem_limit_bytes=40 * 1024 * 1024),
        cost_estimate=cost,
    )(rows, w_gate, w_up, w_down)


def build_kernel(ids_ref, tok_hbm, o_ref, tok_buf, sem):
    copy = pltpu.make_async_copy(tok_hbm, tok_buf, sem)
    copy.start()
    top, tok_rows = ids_ref.shape
    experts, ranks, _ = o_ref.shape
    ids = ids_ref[...]
    expert_col = lax.broadcasted_iota(jnp.int32, (experts, tok_rows), 0)
    present = ids[0:1, :] == expert_col
    for k in range(1, top):
        present = present | (ids[k:k + 1, :] == expert_col)
    earlier = lax.broadcasted_iota(jnp.int32, (tok_rows, tok_rows), 0) < lax.broadcasted_iota(
        jnp.int32, (tok_rows, tok_rows), 1
    )
    before = jnp.dot(
        present.astype(jnp.float32), earlier.astype(jnp.float32), preferred_element_type=jnp.float32
    )
    copy.wait()
    tokens = tok_buf[...]
    for r in range(ranks):
        pick = jnp.where(present & (before == r), 1.0, 0.0).astype(tokens.dtype)
        o_ref[:, r, :] = jnp.dot(pick, tokens, preferred_element_type=jnp.float32).astype(o_ref.dtype)


def build_rows(ids_t, tokens, experts, ranks):
    vmem = pl.BlockSpec(memory_space=pltpu.VMEM)
    return pl.pallas_call(
        build_kernel,
        in_specs=[vmem, pl.BlockSpec(memory_space=pl.ANY)],
        out_specs=vmem,
        out_shape=jax.ShapeDtypeStruct((experts, ranks, tokens.shape[1]), tokens.dtype),
        scratch_shapes=[pltpu.VMEM(tokens.shape, tokens.dtype), pltpu.SemaphoreType.DMA(())],
        compiler_params=pltpu.CompilerParams(vmem_limit_bytes=2 * 1024 * 1024),
    )(ids_t, tokens)


def combine_kernel(w_ref, ret_ref, o_ref):
    tok_rows = o_ref.shape[0]
    experts, ranks, _ = ret_ref.shape
    w = w_ref[...]
    both = None
    for r in range(ranks):
        part = jnp.dot(
            w[:, r * experts:(r + 1) * experts], ret_ref[:, r, :], preferred_element_type=jnp.float32
        )
        both = part if both is None else both + part
    o_ref[...] = (both[:tok_rows] + both[tok_rows:]).astype(o_ref.dtype)


def combine_rows(split, returned, tok_rows):
    vmem = pl.BlockSpec(memory_space=pltpu.VMEM)
    return pl.pallas_call(
        combine_kernel,
        in_specs=[vmem, vmem],
        out_specs=vmem,
        out_shape=jax.ShapeDtypeStruct((tok_rows, returned.shape[2]), returned.dtype),
        compiler_params=pltpu.CompilerParams(vmem_limit_bytes=8 * 1024 * 1024),
    )(split, returned)


def local(tokens, expert_ids, gate_codes, w_gate, w_up, w_down):
    tok_rows, width = tokens.shape
    top = expert_ids.shape[1]
    num_groups = lax.axis_size("group")
    num_local = lax.axis_size("local")
    experts = num_groups * num_local
    capacity = 2 * tok_rows * top // experts
    total_slots = experts * capacity
    outgoing = build_rows(expert_ids.T, tokens, experts, capacity)
    got_rows = lax.all_to_all(outgoing, ("group", "local"), split_axis=0, concat_axis=0, tiled=True)
    expert_ids, got_rows = lax.optimization_barrier((expert_ids, got_rows))
    rows_in = jnp.swapaxes(got_rows, 0, 1).reshape(total_slots, width)
    expert_range = jnp.arange(experts, dtype=jnp.int32)
    onehot = (expert_ids[:, :, None] == expert_range[None, None, :]).astype(jnp.int32)
    present = jnp.sum(onehot, axis=1)
    before = jnp.cumsum(present, axis=0) - present
    slot_rank = jnp.sum(onehot * before[:, None, :], axis=2)
    kept = slot_rank < capacity
    slot_index = jnp.where(kept, slot_rank * experts + expert_ids, total_slots)
    slot_range = jnp.arange(total_slots, dtype=jnp.int32)
    route_hit = slot_index[:, :, None] == slot_range[None, None, :]
    produced = expert_rows(rows_in, w_gate, w_up, w_down)
    returned = lax.all_to_all(produced, ("group", "local"), split_axis=0, concat_axis=0, tiled=True)
    weight = jnp.where(kept, gate_codes.astype(jnp.float32) / 1024.0, jnp.zeros((), jnp.float32))
    combine = jnp.sum(jnp.where(route_hit, weight[:, :, None], 0.0), axis=1)
    combine_hi = lax.reduce_precision(combine, exponent_bits=8, mantissa_bits=7)
    combine_lo = combine - combine_hi
    split = jnp.concatenate([combine_hi, combine_lo], axis=0).astype(jnp.bfloat16)
    return combine_rows(split, returned, tok_rows)


def solution(mesh):
    placed = (
        P(("group", "local"), None),
        P(("group", "local"), None),
        P(("group", "local"), None),
        P(("group", "local"), None, None),
        P(("group", "local"), None, None),
        P(("group", "local"), None, None),
    )
    return jax.shard_map(
        local, mesh=mesh, in_specs=placed, out_specs=P(("group", "local"), None), check_vma=False
    )
```

```python
import jax
import jax.numpy as jnp
from jax import lax
from jax.experimental import pallas as pl
from jax.experimental.pallas import tpu as pltpu
from jax.sharding import PartitionSpec as P

H_BLOCK = 256


def mlp_kernel(x_ref, wg_ref, wu_hbm, wd_hbm, o_ref, wu_buf, wd_all, hid_ref, sems):
    steps = wg_ref.shape[2] // H_BLOCK

    def fetch_up(j):
        cols = pl.ds(j * H_BLOCK, H_BLOCK)
        return pltpu.make_async_copy(wu_hbm.at[0, :, cols], wu_buf.at[j % 2], sems.at[0, j % 2])

    def fetch_down(j):
        rows = pl.ds(j * H_BLOCK, H_BLOCK)
        return pltpu.make_async_copy(wd_hbm.at[0, rows, :], wd_all.at[rows, :], sems.at[1, j])

    x = x_ref[...]
    up_next = fetch_up(0)
    up_next.start()
    downs = []
    for j in range(steps):
        up_now = up_next
        if j + 1 < steps:
            up_next = fetch_up(j + 1)
            up_next.start()
        downs.append(fetch_down(j))
        downs[-1].start()
        up_now.wait()
        cols = pl.ds(j * H_BLOCK, H_BLOCK)
        gate_part = jnp.dot(x, wg_ref[0, :, cols], preferred_element_type=jnp.float32)
        up_part = jnp.dot(x, wu_buf[j % 2], preferred_element_type=jnp.float32)
        hid_ref[:, cols] = (gate_part / (1.0 + jnp.exp(-gate_part)) * up_part).astype(jnp.bfloat16)
    for c in downs:
        c.wait()
    half = hid_ref.shape[0] // 2
    wd = wd_all[...]
    for r in range(2):
        acc = jnp.dot(hid_ref[r * half:(r + 1) * half, :], wd, preferred_element_type=jnp.float32)
        o_ref[:, r, :] = acc.astype(o_ref.dtype)


def expert_rows(rows, w_gate, w_up, w_down):
    slots, width = rows.shape
    hid = w_gate.shape[2]
    cost = pl.CostEstimate(
        flops=6 * slots * width * hid,
        transcendentals=slots * hid,
        bytes_accessed=2 * (3 * width * hid + 2 * slots * width),
    )
    vmem = pl.BlockSpec(memory_space=pltpu.VMEM)
    anyspace = pl.BlockSpec(memory_space=pl.ANY)
    return pl.pallas_call(
        mlp_kernel,
        in_specs=[vmem, vmem, anyspace, anyspace],
        out_specs=vmem,
        out_shape=jax.ShapeDtypeStruct((slots // 2, 2, width), jnp.bfloat16),
        scratch_shapes=[
            pltpu.VMEM((2, width, H_BLOCK), jnp.bfloat16),
            pltpu.VMEM((hid, width), jnp.bfloat16),
            pltpu.VMEM((slots, hid), jnp.bfloat16),
            pltpu.SemaphoreType.DMA((2, hid // H_BLOCK)),
        ],
        compiler_params=pltpu.CompilerParams(vmem_limit_bytes=40 * 1024 * 1024),
        cost_estimate=cost,
    )(rows, w_gate, w_up, w_down)


def build_kernel(ids_ref, tok_hbm, o_ref, tok_buf, sem):
    copy = pltpu.make_async_copy(tok_hbm, tok_buf, sem)
    copy.start()
    top, tok_rows = ids_ref.shape
    experts, ranks, _ = o_ref.shape
    ids = ids_ref[...]
    expert_col = lax.broadcasted_iota(jnp.int32, (experts, tok_rows), 0)
    present = ids[0:1, :] == expert_col
    for k in range(1, top):
        present = present | (ids[k:k + 1, :] == expert_col)
    earlier = lax.broadcasted_iota(jnp.int32, (tok_rows, tok_rows), 0) < lax.broadcasted_iota(
        jnp.int32, (tok_rows, tok_rows), 1
    )
    before = jnp.dot(
        present.astype(jnp.float32), earlier.astype(jnp.float32), preferred_element_type=jnp.float32
    )
    copy.wait()
    tokens = tok_buf[...]
    for r in range(ranks):
        pick = jnp.where(present & (before == r), 1.0, 0.0).astype(tokens.dtype)
        o_ref[:, r, :] = jnp.dot(pick, tokens, preferred_element_type=jnp.float32).astype(o_ref.dtype)


def build_rows(ids_t, tokens, experts, ranks):
    vmem = pl.BlockSpec(memory_space=pltpu.VMEM)
    return pl.pallas_call(
        build_kernel,
        in_specs=[vmem, pl.BlockSpec(memory_space=pl.ANY)],
        out_specs=vmem,
        out_shape=jax.ShapeDtypeStruct((experts, ranks, tokens.shape[1]), tokens.dtype),
        scratch_shapes=[pltpu.VMEM(tokens.shape, tokens.dtype), pltpu.SemaphoreType.DMA(())],
        compiler_params=pltpu.CompilerParams(vmem_limit_bytes=2 * 1024 * 1024),
    )(ids_t, tokens)


def local(tokens, expert_ids, gate_codes, w_gate, w_up, w_down):
    tok_rows, width = tokens.shape
    top = expert_ids.shape[1]
    num_groups = lax.axis_size("group")
    num_local = lax.axis_size("local")
    experts = num_groups * num_local
    capacity = 2 * tok_rows * top // experts
    total_slots = experts * capacity
    outgoing = build_rows(expert_ids.T, tokens, experts, capacity)
    got_rows = lax.all_to_all(outgoing, ("group", "local"), split_axis=0, concat_axis=0, tiled=True)
    expert_ids, got_rows = lax.optimization_barrier((expert_ids, got_rows))
    rows_in = jnp.swapaxes(got_rows, 0, 1).reshape(total_slots, width)
    expert_range = jnp.arange(experts, dtype=jnp.int32)
    onehot = (expert_ids[:, :, None] == expert_range[None, None, :]).astype(jnp.int32)
    present = jnp.sum(onehot, axis=1)
    before = jnp.cumsum(present, axis=0) - present
    slot_rank = jnp.sum(onehot * before[:, None, :], axis=2)
    kept = slot_rank < capacity
    slot_index = jnp.where(kept, slot_rank * experts + expert_ids, total_slots)
    slot_range = jnp.arange(total_slots, dtype=jnp.int32)
    route_hit = slot_index[:, :, None] == slot_range[None, None, :]
    produced = expert_rows(rows_in, w_gate, w_up, w_down)
    returned = lax.all_to_all(produced, ("group", "local"), split_axis=0, concat_axis=0, tiled=True)
    back_flat = jnp.swapaxes(returned, 0, 1).reshape(total_slots, width)
    weight = jnp.where(kept, gate_codes.astype(jnp.float32) / 1024.0, jnp.zeros((), jnp.float32))
    combine = jnp.sum(jnp.where(route_hit, weight[:, :, None], 0.0), axis=1)
    combine_hi = lax.reduce_precision(combine, exponent_bits=8, mantissa_bits=7)
    combine_lo = combine - combine_hi
    split = jnp.concatenate([combine_hi, combine_lo], axis=0).astype(jnp.bfloat16)
    both = jnp.dot(split, back_flat, preferred_element_type=jnp.float32)
    mixed = both[:tok_rows] + both[tok_rows:]
    return mixed.astype(jnp.bfloat16)


def solution(mesh):
    placed = (
        P(("group", "local"), None),
        P(("group", "local"), None),
        P(("group", "local"), None),
        P(("group", "local"), None, None),
        P(("group", "local"), None, None),
        P(("group", "local"), None, None),
    )
    return jax.shard_map(
        local, mesh=mesh, in_specs=placed, out_specs=P(("group", "local"), None), check_vma=False
    )
```

```python
import jax
import jax.numpy as jnp
from jax import lax
from jax.experimental import pallas as pl
from jax.experimental.pallas import tpu as pltpu
from jax.sharding import PartitionSpec as P

H_BLOCK = 256


def mlp_kernel(x_ref, wg_ref, wu_hbm, wd_hbm, o_ref, wu_buf, wd_all, hid_ref, sems):
    steps = wg_ref.shape[2] // H_BLOCK

    def fetch_up(j):
        cols = pl.ds(j * H_BLOCK, H_BLOCK)
        return pltpu.make_async_copy(wu_hbm.at[0, :, cols], wu_buf.at[j % 2], sems.at[0, j % 2])

    def fetch_down(j):
        rows = pl.ds(j * H_BLOCK, H_BLOCK)
        return pltpu.make_async_copy(wd_hbm.at[0, rows, :], wd_all.at[rows, :], sems.at[1, j])

    x = x_ref[...]
    up_next = fetch_up(0)
    up_next.start()
    downs = []
    for j in range(steps):
        up_next.wait()
        if j + 1 < steps:
            up_next = fetch_up(j + 1)
            up_next.start()
        downs.append(fetch_down(j))
        downs[-1].start()
        cols = pl.ds(j * H_BLOCK, H_BLOCK)
        gate_part = jnp.dot(x, wg_ref[0, :, cols], preferred_element_type=jnp.float32)
        up_part = jnp.dot(x, wu_buf[j % 2], preferred_element_type=jnp.float32)
        hid_ref[:, cols] = (gate_part / (1.0 + jnp.exp(-gate_part)) * up_part).astype(jnp.bfloat16)
    for c in downs:
        c.wait()
    acc = jnp.dot(hid_ref[...], wd_all[...], preferred_element_type=jnp.float32)
    half = acc.shape[0] // 2
    for r in range(2):
        o_ref[:, r, :] = acc[r * half:(r + 1) * half].astype(o_ref.dtype)


def expert_rows(rows, w_gate, w_up, w_down):
    slots, width = rows.shape
    hid = w_gate.shape[2]
    cost = pl.CostEstimate(
        flops=6 * slots * width * hid,
        transcendentals=slots * hid,
        bytes_accessed=2 * (3 * width * hid + 2 * slots * width),
    )
    vmem = pl.BlockSpec(memory_space=pltpu.VMEM)
    anyspace = pl.BlockSpec(memory_space=pl.ANY)
    return pl.pallas_call(
        mlp_kernel,
        in_specs=[vmem, vmem, anyspace, anyspace],
        out_specs=vmem,
        out_shape=jax.ShapeDtypeStruct((slots // 2, 2, width), jnp.bfloat16),
        scratch_shapes=[
            pltpu.VMEM((2, width, H_BLOCK), jnp.bfloat16),
            pltpu.VMEM((hid, width), jnp.bfloat16),
            pltpu.VMEM((slots, hid), jnp.bfloat16),
            pltpu.SemaphoreType.DMA((2, hid // H_BLOCK)),
        ],
        compiler_params=pltpu.CompilerParams(vmem_limit_bytes=40 * 1024 * 1024),
        cost_estimate=cost,
    )(rows, w_gate, w_up, w_down)


def build_kernel(ids_ref, tok_hbm, o_ref, tok_buf, sem):
    copy = pltpu.make_async_copy(tok_hbm, tok_buf, sem)
    copy.start()
    top, tok_rows = ids_ref.shape
    experts, ranks, _ = o_ref.shape
    ids = ids_ref[...]
    expert_col = lax.broadcasted_iota(jnp.int32, (experts, tok_rows), 0)
    present = ids[0:1, :] == expert_col
    for k in range(1, top):
        present = present | (ids[k:k + 1, :] == expert_col)
    earlier = lax.broadcasted_iota(jnp.int32, (tok_rows, tok_rows), 0) < lax.broadcasted_iota(
        jnp.int32, (tok_rows, tok_rows), 1
    )
    before = jnp.dot(
        present.astype(jnp.float32), earlier.astype(jnp.float32), preferred_element_type=jnp.float32
    )
    copy.wait()
    tokens = tok_buf[...]
    for r in range(ranks):
        pick = jnp.where(present & (before == r), 1.0, 0.0).astype(tokens.dtype)
        o_ref[:, r, :] = jnp.dot(pick, tokens, preferred_element_type=jnp.float32).astype(o_ref.dtype)


def build_rows(ids_t, tokens, experts, ranks):
    vmem = pl.BlockSpec(memory_space=pltpu.VMEM)
    return pl.pallas_call(
        build_kernel,
        in_specs=[vmem, pl.BlockSpec(memory_space=pl.ANY)],
        out_specs=vmem,
        out_shape=jax.ShapeDtypeStruct((experts, ranks, tokens.shape[1]), tokens.dtype),
        scratch_shapes=[pltpu.VMEM(tokens.shape, tokens.dtype), pltpu.SemaphoreType.DMA(())],
        compiler_params=pltpu.CompilerParams(vmem_limit_bytes=2 * 1024 * 1024),
    )(ids_t, tokens)


def local(tokens, expert_ids, gate_codes, w_gate, w_up, w_down):
    tok_rows, width = tokens.shape
    top = expert_ids.shape[1]
    num_groups = lax.axis_size("group")
    num_local = lax.axis_size("local")
    experts = num_groups * num_local
    capacity = 2 * tok_rows * top // experts
    total_slots = experts * capacity
    outgoing = build_rows(expert_ids.T, tokens, experts, capacity)
    got_rows = lax.all_to_all(outgoing, ("group", "local"), split_axis=0, concat_axis=0, tiled=True)
    expert_ids, got_rows = lax.optimization_barrier((expert_ids, got_rows))
    rows_in = jnp.swapaxes(got_rows, 0, 1).reshape(total_slots, width)
    expert_range = jnp.arange(experts, dtype=jnp.int32)
    onehot = (expert_ids[:, :, None] == expert_range[None, None, :]).astype(jnp.int32)
    present = jnp.sum(onehot, axis=1)
    before = jnp.cumsum(present, axis=0) - present
    slot_rank = jnp.sum(onehot * before[:, None, :], axis=2)
    kept = slot_rank < capacity
    slot_index = jnp.where(kept, slot_rank * experts + expert_ids, total_slots)
    slot_range = jnp.arange(total_slots, dtype=jnp.int32)
    route_hit = slot_index[:, :, None] == slot_range[None, None, :]
    produced = expert_rows(rows_in, w_gate, w_up, w_down)
    returned = lax.all_to_all(produced, ("group", "local"), split_axis=0, concat_axis=0, tiled=True)
    back_flat = jnp.swapaxes(returned, 0, 1).reshape(total_slots, width)
    weight = jnp.where(kept, gate_codes.astype(jnp.float32) / 1024.0, jnp.zeros((), jnp.float32))
    combine = jnp.sum(jnp.where(route_hit, weight[:, :, None], 0.0), axis=1)
    combine_hi = lax.reduce_precision(combine, exponent_bits=8, mantissa_bits=7)
    combine_lo = combine - combine_hi
    split = jnp.concatenate([combine_hi, combine_lo], axis=0).astype(jnp.bfloat16)
    both = jnp.dot(split, back_flat, preferred_element_type=jnp.float32)
    mixed = both[:tok_rows] + both[tok_rows:]
    return mixed.astype(jnp.bfloat16)


def solution(mesh):
    placed = (
        P(("group", "local"), None),
        P(("group", "local"), None),
        P(("group", "local"), None),
        P(("group", "local"), None, None),
        P(("group", "local"), None, None),
        P(("group", "local"), None, None),
    )
    return jax.shard_map(
        local, mesh=mesh, in_specs=placed, out_specs=P(("group", "local"), None), check_vma=False
    )
```
